512 devices in a mesh: row: 16 (over x_hi, y, core), col: 32 (over z, x_lo).
Axes of the slice: x: 4 (x_hi: 2, x_lo: 2; x = x_hi * 2 + x_lo), y: 4, z: 16, core: 2. Of those that a mesh axis runs over, the one named last changes fastest.
Arguments:
- probes: bfloat16 [512, 262144], P(None, ('row', 'col')), may hold values from -6 to 6
- own_blocks: bfloat16 [3, 262144, 512], P(None, ('row', 'col')), may hold values from -0.1875 to 0.1875
- cross_blocks: bfloat16 [3, 262144, 512], P(None, ('row', 'col')), may hold values from -0.1875 to 0.1875
- level_perm: int32 [3, 262144], P(None, ('row', 'col')), may hold values from 0 to 511, as said below
Outputs:
- mixed: bfloat16 [512, 262144], P(None, ('row', 'col'))
The draws below stay inside these ranges and needn't reach their ends.
Inputs may be any that keep to these rules, and one draw needn't show every extreme that they name: `level_perm`: each aligned run of 512 entries of a level is a permutation of 0 to 511.
All inputs are finite; a program needn't handle non-finite values.
Results may differ from the reference program's by a relative error of at most 0.0057.
Values may be sent and summed in bfloat16 or wider, within the bound.
No kernel may reach another device: no remote copies, remote signals or barrier semaphores. Data moves between devices by JAX's collectives and lax.ppermute only.
A program may use at most 64 MiB of HBM per device.

```python
import jax
import jax.numpy as jnp
from jax import lax

BR = 512
PROBES = 512
LEVELS = 3
BLOCKS = 512
NK = 262144
N_ROW = 16
N_COL = 32


def draw_level_perm(key, part):
    keys = jax.random.split(jax.random.fold_in(key, 17), LEVELS * BLOCKS)
    perms = jax.vmap(lambda k: jax.random.permutation(k, BR))(keys)
    return perms.reshape(LEVELS, BLOCKS * BR).astype(jnp.int32)


def steps_of(rng, extent, cuts, least, top_value):
    factor_of = 1.0
    for dim, blocks in cuts:
        draws = jax.random.uniform(jax.random.fold_in(jax.random.fold_in(rng, 6), dim), (blocks,), jnp.float32, least / len(cuts), top_value / len(cuts))
        factor_of = factor_of * jnp.repeat(jnp.exp(draws), extent[dim] // blocks).reshape((-1,) + (1,) * (len(extent) - 1 - dim))
    return factor_of


def bell_draw(own_key, extent, spread, bound, cuts=(), kind=jnp.bfloat16):
    array = jax.random.normal(own_key, extent, jnp.float32) * spread
    if len(cuts) > 0:
        array = steps_of(own_key, extent, cuts, -0.22, 0.18) * array
    return jnp.clip(array, min=-bound, max=bound).astype(kind)


def setup_inputs(seed: int = 0) -> dict:
    streams_of = jax.random.split(jax.random.key(seed), 5)
    probes = bell_draw(streams_of[0], (PROBES, NK), 1.0, 6.0, ((1, 512),))
    own_blocks = bell_draw(streams_of[1], (LEVELS, NK, BR), (2 * BR) ** -0.5, 0.1875, ((1, 512),))
    cross_blocks = bell_draw(streams_of[2], (LEVELS, NK, BR), (2 * BR) ** -0.5, 0.1875, ((1, 512),))
    level_perm = draw_level_perm(jax.random.fold_in(streams_of[4], 71), 0)
    return {"probes": probes, "own_blocks": own_blocks, "cross_blocks": cross_blocks, "level_perm": level_perm}


def reference(probes, own_blocks, cross_blocks, level_perm):
    ncol_bits = N_COL.bit_length() - 1
    nrow_bits = N_ROW.bit_length() - 1
    bits = [ncol_bits - 1, ncol_bits + nrow_bits - 1, 0]
    panel = probes.reshape(PROBES, BLOCKS, BR).transpose(1, 0, 2)
    index = jnp.arange(BLOCKS, dtype=jnp.int32)
    for level in range(LEVELS):
        partner_index = jnp.bitwise_xor(index, jnp.int32(1 << bits[level]))
        partner = panel[partner_index]
        own = own_blocks[level].reshape(BLOCKS, BR, BR)
        cross = cross_blocks[level].reshape(BLOCKS, BR, BR)
        order = level_perm[level].reshape(BLOCKS, BR)

        def one_block(items):
            mine, other, own_b, cross_b, order_b = items
            total = jnp.dot(mine, own_b, preferred_element_type=jnp.float32)
            total = total + jnp.dot(other, cross_b, preferred_element_type=jnp.float32)
            return jnp.take(total, order_b, axis=1).astype(jnp.bfloat16)

        panel = lax.map(one_block, (panel, partner, own, cross, order))
    return panel.transpose(1, 0, 2).reshape(PROBES, NK)
```

```python
import jax
import jax.numpy as jnp
from jax import lax
from jax.sharding import PartitionSpec as P

CHUNKS = 2


def from_partner(value, axis, distance):
    mask = 2**distance
    pairs = [(source, source ^ mask) for source in range(lax.axis_size(axis))]
    return lax.ppermute(value, axis, pairs)


def permuted_columns(weights, order):
    n = weights.shape[-1]
    onehot = (lax.broadcasted_iota(jnp.int32, (n, n), 0) == order[None, :]).astype(weights.dtype)
    return jnp.dot(weights, onehot, preferred_element_type=jnp.float32).astype(weights.dtype)


def per_device(probes, own_blocks, cross_blocks, level_perm):
    col_bits = lax.axis_size("col").bit_length() - 1
    row_bits = lax.axis_size("row").bit_length() - 1
    plan = [("col", col_bits - 1), ("row", row_bits - 1), ("col", 0)]
    br = own_blocks.shape[1]
    weights = []
    for level in range(3):
        both = jnp.concatenate([own_blocks[level], cross_blocks[level]], axis=0)
        both = permuted_columns(both, level_perm[level])
        weights.append((both[:br], both[br:]))
    rows = probes.shape[0] // CHUNKS
    outs = []
    for chunk in range(CHUNKS):
        panel = probes[chunk * rows:(chunk + 1) * rows]
        for level, (axis, bit) in enumerate(plan):
            own, cross = weights[level]
            other = from_partner(panel, axis, bit)
            total = jnp.dot(panel, own, preferred_element_type=jnp.float32)
            total = total + jnp.dot(other, cross, preferred_element_type=jnp.float32)
            panel = total.astype(jnp.bfloat16)
        outs.append(panel)
    return jnp.concatenate(outs, axis=0)


def solution(mesh):
    placed = (
        P(None, ("row", "col")),
        P(None, ("row", "col"), None),
        P(None, ("row", "col"), None),
        P(None, ("row", "col")),
    )
    return jax.shard_map(
        per_device, mesh=mesh, in_specs=placed, out_specs=P(None, ("row", "col")), check_vma=False
    )
```

```python
import jax
import jax.numpy as jnp
from jax import lax
from jax.sharding import PartitionSpec as P

CHUNKS = 2


def from_partner(value, axis, distance):
    mask = 2**distance
    pairs = [(source, source ^ mask) for source in range(lax.axis_size(axis))]
    return lax.ppermute(value, axis, pairs)


def shifted(value, axis, step):
    size = lax.axis_size(axis)
    pairs = [(source, (source + step) % size) for source in range(size)]
    return lax.ppermute(value, axis, pairs)


def permuted_columns(weights, order):
    n = weights.shape[-1]
    onehot = (lax.broadcasted_iota(jnp.int32, (n, n), 0) == order[None, :]).astype(weights.dtype)
    return jnp.dot(weights, onehot, preferred_element_type=jnp.float32).astype(weights.dtype)


def per_device(probes, own_blocks, cross_blocks, level_perm):
    col_bits = lax.axis_size("col").bit_length() - 1
    row_bits = lax.axis_size("row").bit_length() - 1
    plan = [("col", col_bits - 1), ("row", row_bits - 1), ("col", 0)]
    br = own_blocks.shape[1]
    weights = []
    for level in range(3):
        both = jnp.concatenate([own_blocks[level], cross_blocks[level]], axis=0)
        both = permuted_columns(both, level_perm[level])
        weights.append((both[:br], both[br:]))
    rows = probes.shape[0] // CHUNKS
    outs = []
    for chunk in range(CHUNKS):
        panel = probes[chunk * rows:(chunk + 1) * rows]
        for level, (axis, bit) in enumerate(plan):
            own, cross = weights[level]
            if level == 0:
                step = (2**bit // 2) * (1 if chunk % 2 == 0 else -1)
                other = shifted(shifted(panel, axis, step), axis, step)
            else:
                other = from_partner(panel, axis, bit)
            total = jnp.dot(panel, own, preferred_element_type=jnp.float32)
            total = total + jnp.dot(other, cross, preferred_element_type=jnp.float32)
            panel = total.astype(jnp.bfloat16)
        outs.append(panel)
    return jnp.concatenate(outs, axis=0)


def solution(mesh):
    placed = (
        P(None, ("row", "col")),
        P(None, ("row", "col"), None),
        P(None, ("row", "col"), None),
        P(None, ("row", "col")),
    )
    return jax.shard_map(
        per_device, mesh=mesh, in_specs=placed, out_specs=P(None, ("row", "col")), check_vma=False
    )
```

```python
import jax
import jax.numpy as jnp
from jax import lax
from jax.sharding import PartitionSpec as P

CHUNKS = 2


def from_partner(value, axis, distance):
    mask = 2**distance
    pairs = [(source, source ^ mask) for source in range(lax.axis_size(axis))]
    return lax.ppermute(value, axis, pairs)


def permuted_columns(weights, order):
    n = weights.shape[-1]
    onehot = (lax.broadcasted_iota(jnp.int32, (n, n), 0) == order[None, :]).astype(weights.dtype)
    return jnp.dot(weights, onehot, preferred_element_type=jnp.float32).astype(weights.dtype)


def per_device(probes, own_blocks, cross_blocks, level_perm):
    col_bits = lax.axis_size("col").bit_length() - 1
    row_bits = lax.axis_size("row").bit_length() - 1
    plan = [("col", col_bits - 1), ("row", row_bits - 1), ("col", 0)]
    br = own_blocks.shape[1]
    weights = []
    for level in range(3):
        both = jnp.concatenate([own_blocks[level], cross_blocks[level]], axis=0)
        both = permuted_columns(both, level_perm[level])
        weights.append((both[:br], both[br:]))
    rows = probes.shape[0] // CHUNKS
    arrived = from_partner(probes, *plan[0])
    panels, others = [], []
    for chunk in range(CHUNKS):
        part = slice(chunk * rows, (chunk + 1) * rows)
        panel = probes[part]
        for level, (axis, bit) in enumerate(plan):
            own, cross = weights[level]
            if level == 0:
                other = arrived[part]
            else:
                other = from_partner(panel, axis, bit)
            if level == 2:
                break
            total = jnp.dot(panel, own, preferred_element_type=jnp.float32)
            total = total + jnp.dot(other, cross, preferred_element_type=jnp.float32)
            panel = total.astype(jnp.bfloat16)
        panels.append(panel)
        others.append(other)
    own, cross = weights[2]
    total = jnp.dot(jnp.concatenate(panels), own, preferred_element_type=jnp.float32)
    total = total + jnp.dot(jnp.concatenate(others), cross, preferred_element_type=jnp.float32)
    return total.astype(jnp.bfloat16)


def solution(mesh):
    placed = (
        P(None, ("row", "col")),
        P(None, ("row", "col"), None),
        P(None, ("row", "col"), None),
        P(None, ("row", "col")),
    )
    return jax.shard_map(
        per_device, mesh=mesh, in_specs=placed, out_specs=P(None, ("row", "col")), check_vma=False
    )
```

```python
import jax
import jax.numpy as jnp
from jax import lax
from jax.sharding import PartitionSpec as P

CHUNKS = 2


def from_partner(value, axis, distance):
    mask = 2**distance
    pairs = [(source, source ^ mask) for source in range(lax.axis_size(axis))]
    return lax.ppermute(value, axis, pairs)


def permuted_columns(weights, order):
    n = weights.shape[-1]
    onehot = (lax.broadcasted_iota(jnp.int32, (n, n), 0) == order[None, :]).astype(weights.dtype)
    return jnp.dot(weights, onehot, preferred_element_type=jnp.float32).astype(weights.dtype)


def per_device(probes, own_blocks, cross_blocks, level_perm):
    col_bits = lax.axis_size("col").bit_length() - 1
    row_bits = lax.axis_size("row").bit_length() - 1
    plan = [("col", col_bits - 1), ("row", row_bits - 1), ("col", 0)]
    br = own_blocks.shape[1]
    weights = []
    for level in range(3):
        both = jnp.concatenate([own_blocks[level], cross_blocks[level]], axis=0)
        both = permuted_columns(both, level_perm[level])
        weights.append((both[:br], both[br:]))
    rows = probes.shape[0] // CHUNKS
    panels = [probes[chunk * rows:(chunk + 1) * rows] for chunk in range(CHUNKS)]
    arrived = [from_partner(panels[0], *plan[0])]
    outs = []
    for chunk in range(CHUNKS):
        panel = panels[chunk]
        for level, (axis, bit) in enumerate(plan):
            own, cross = weights[level]
            if level == 0:
                other = arrived[chunk]
            else:
                other = from_partner(panel, axis, bit)
            if level == 2 and chunk + 1 < CHUNKS:
                other, arrived[chunk + 1] = lax.optimization_barrier((other, arrived[chunk + 1]))
            total = jnp.dot(panel, own, preferred_element_type=jnp.float32)
            total = total + jnp.dot(other, cross, preferred_element_type=jnp.float32)
            panel = total.astype(jnp.bfloat16)
            if level == 0 and chunk + 1 < CHUNKS:
                panel, after = lax.optimization_barrier((panel, panels[chunk + 1]))
                arrived.append(from_partner(after, *plan[0]))
        outs.append(panel)
    return jnp.concatenate(outs, axis=0)


def solution(mesh):
    placed = (
        P(None, ("row", "col")),
        P(None, ("row", "col"), None),
        P(None, ("row", "col"), None),
        P(None, ("row", "col")),
    )
    return jax.shard_map(
        per_device, mesh=mesh, in_specs=placed, out_specs=P(None, ("row", "col")), check_vma=False
    )
```

```python
import jax
import jax.numpy as jnp
from jax import lax
from jax.sharding import PartitionSpec as P

CHUNKS = 2


def from_partner(value, axis, distance):
    mask = 2**distance
    pairs = [(source, source ^ mask) for source in range(lax.axis_size(axis))]
    return lax.ppermute(value, axis, pairs)


def shifted(value, axis, step):
    size = lax.axis_size(axis)
    pairs = [(source, (source + step) % size) for source in range(size)]
    return lax.ppermute(value, axis, pairs)


def permuted_columns(weights, order):
    n = weights.shape[-1]
    onehot = (lax.broadcasted_iota(jnp.int32, (n, n), 0) == order[None, :]).astype(weights.dtype)
    return jnp.dot(weights, onehot, preferred_element_type=jnp.float32).astype(weights.dtype)


def per_device(probes, own_blocks, cross_blocks, level_perm):
    col_bits = lax.axis_size("col").bit_length() - 1
    row_bits = lax.axis_size("row").bit_length() - 1
    plan = [("col", col_bits - 1), ("row", row_bits - 1), ("col", 0)]
    br = own_blocks.shape[1]
    weights = []
    for level in range(3):
        both = jnp.concatenate([own_blocks[level], cross_blocks[level]], axis=0)
        both = permuted_columns(both, level_perm[level])
        weights.append((both[:br], both[br:]))
    rows = probes.shape[0] // CHUNKS
    outs = []
    for chunk in range(CHUNKS):
        panel = probes[chunk * rows:(chunk + 1) * rows]
        for level, (axis, bit) in enumerate(plan):
            own, cross = weights[level]
            if level == 0 and chunk % 2 == 1:
                step = -(2**bit // 2)
                other = shifted(shifted(panel, axis, step), axis, step)
            else:
                other = from_partner(panel, axis, bit)
            total = jnp.dot(panel, own, preferred_element_type=jnp.float32)
            total = total + jnp.dot(other, cross, preferred_element_type=jnp.float32)
            panel = total.astype(jnp.bfloat16)
        outs.append(panel)
    return jnp.concatenate(outs, axis=0)


def solution(mesh):
    placed = (
        P(None, ("row", "col")),
        P(None, ("row", "col"), None),
        P(None, ("row", "col"), None),
        P(None, ("row", "col")),
    )
    return jax.shard_map(
        per_device, mesh=mesh, in_specs=placed, out_specs=P(None, ("row", "col")), check_vma=False
    )
```

```python
import jax
import jax.numpy as jnp
from jax import lax
from jax.sharding import PartitionSpec as P

CHUNKS = 2


def from_partner(value, axis, distance):
    mask = 2**distance
    pairs = [(source, source ^ mask) for source in range(lax.axis_size(axis))]
    return lax.ppermute(value, axis, pairs)


def permuted_columns(weights, order):
    n = weights.shape[-1]
    onehot = (lax.broadcasted_iota(jnp.int32, (n, n), 0) == order[None, :]).astype(weights.dtype)
    return jnp.dot(weights, onehot, preferred_element_type=jnp.float32).astype(weights.dtype)


def per_device(probes, own_blocks, cross_blocks, level_perm):
    col_bits = lax.axis_size("col").bit_length() - 1
    row_bits = lax.axis_size("row").bit_length() - 1
    plan = [("col", col_bits - 1), ("row", row_bits - 1), ("col", 0)]
    br = own_blocks.shape[1]
    weights = []
    for level in range(3):
        both = jnp.concatenate([own_blocks[level], cross_blocks[level]], axis=0)
        both = permuted_columns(both, level_perm[level])
        weights.append((both[:br], both[br:]))
    rows = probes.shape[0] // CHUNKS
    panels = [probes[chunk * rows:(chunk + 1) * rows] for chunk in range(CHUNKS)]
    weights, panels[1:] = lax.optimization_barrier((weights, panels[1:]))
    outs = []
    for chunk in range(CHUNKS):
        panel = panels[chunk]
        for level, (axis, bit) in enumerate(plan):
            own, cross = weights[level]
            other = from_partner(panel, axis, bit)
            total = jnp.dot(panel, own, preferred_element_type=jnp.float32)
            total = total + jnp.dot(other, cross, preferred_element_type=jnp.float32)
            panel = total.astype(jnp.bfloat16)
        outs.append(panel)
    return jnp.concatenate(outs, axis=0)


def solution(mesh):
    placed = (
        P(None, ("row", "col")),
        P(None, ("row", "col"), None),
        P(None, ("row", "col"), None),
        P(None, ("row", "col")),
    )
    return jax.shard_map(
        per_device, mesh=mesh, in_specs=placed, out_specs=P(None, ("row", "col")), check_vma=False
    )
```

```python
import jax
import jax.numpy as jnp
from jax import lax
from jax.sharding import PartitionSpec as P

CHUNKS = 2


def from_partner(value, axis, distance):
    mask = 2**distance
    pairs = [(source, source ^ mask) for source in range(lax.axis_size(axis))]
    return lax.ppermute(value, axis, pairs)


def from_diagonal(value, row_bit, col_bit):
    rows, cols = lax.axis_size("row"), lax.axis_size("col")
    pairs = [
        (r * cols + c, (r ^ 2**row_bit) * cols + (c ^ 2**col_bit)) for r in range(rows) for c in range(cols)
    ]
    return lax.ppermute(value, ("row", "col"), pairs)


def permuted_columns(weights, order):
    n = weights.shape[-1]
    onehot = (lax.broadcasted_iota(jnp.int32, (n, n), 0) == order[None, :]).astype(weights.dtype)
    return jnp.dot(weights, onehot, preferred_element_type=jnp.float32).astype(weights.dtype)


def split(product):
    high = product.astype(jnp.bfloat16)
    low = (product - high.astype(jnp.float32)).astype(jnp.bfloat16)
    return high, low


def times(panel, pair):
    high, low = pair
    total = jnp.dot(panel, high, preferred_element_type=jnp.float32)
    return total + jnp.dot(panel, low, preferred_element_type=jnp.float32)


def product(a, b):
    return jnp.dot(a, b, preferred_element_type=jnp.float32)


def per_device(probes, own_blocks, cross_blocks, level_perm):
    col_bits = lax.axis_size("col").bit_length() - 1
    row_bits = lax.axis_size("row").bit_length() - 1
    z_bit, hi_bit, lo_bit = col_bits - 1, row_bits - 1, 0
    br = own_blocks.shape[1]
    weights = []
    for level in range(3):
        both = jnp.concatenate([own_blocks[level], cross_blocks[level]], axis=0)
        both = permuted_columns(both, level_perm[level])
        weights.append((both[:br], both[br:]))
    (own0, cross0), (own1, cross1), (own2, cross2) = weights
    theirs = from_partner(jnp.stack([cross2, cross1, own2]), "col", lo_bit)
    k_self = split(product(own1, own2))
    k_diag = split(product(theirs[1], cross2))
    k_to_p = split(product(own1, theirs[0]))
    k_diag_p = split(product(theirs[1], theirs[2]))
    rows = probes.shape[0] // CHUNKS
    outs = []
    for chunk in range(CHUNKS):
        panel = probes[chunk * rows:(chunk + 1) * rows]
        other = from_partner(panel, "col", z_bit)
        total = jnp.dot(panel, own0, preferred_element_type=jnp.float32)
        total = total + jnp.dot(other, cross0, preferred_element_type=jnp.float32)
        panel = total.astype(jnp.bfloat16)
        diag = from_diagonal(panel, hi_bit, lo_bit)
        share = (times(panel, k_to_p) + times(diag, k_diag_p)).astype(jnp.bfloat16)
        received = from_partner(share, "col", lo_bit)
        total = times(panel, k_self) + times(diag, k_diag)
        outs.append((total + received.astype(jnp.float32)).astype(jnp.bfloat16))
    return jnp.concatenate(outs, axis=0)


def solution(mesh):
    placed = (
        P(None, ("row", "col")),
        P(None, ("row", "col"), None),
        P(None, ("row", "col"), None),
        P(None, ("row", "col")),
    )
    return jax.shard_map(
        per_device, mesh=mesh, in_specs=placed, out_specs=P(None, ("row", "col")), check_vma=False
    )
```

```python
import jax
import jax.numpy as jnp
from jax import lax
from jax.sharding import PartitionSpec as P

CHUNKS = 2


def from_partner(value, axis, distance):
    mask = 2**distance
    pairs = [(source, source ^ mask) for source in range(lax.axis_size(axis))]
    return lax.ppermute(value, axis, pairs)


def from_diagonal(value, row_bit, col_bit):
    rows, cols = lax.axis_size("row"), lax.axis_size("col")
    pairs = [
        (r * cols + c, (r ^ 2**row_bit) * cols + (c ^ 2**col_bit)) for r in range(rows) for c in range(cols)
    ]
    return lax.ppermute(value, ("row", "col"), pairs)


def permuted_columns(weights, order):
    n = weights.shape[-1]
    onehot = (lax.broadcasted_iota(jnp.int32, (n, n), 0) == order[None, :]).astype(weights.dtype)
    return jnp.dot(weights, onehot, preferred_element_type=jnp.float32).astype(weights.dtype)


def split(product):
    high = product.astype(jnp.bfloat16)
    low = (product - high.astype(jnp.float32)).astype(jnp.bfloat16)
    return high, low


def times(panel, pair):
    high, low = pair
    total = jnp.dot(panel, high, preferred_element_type=jnp.float32)
    return total + jnp.dot(panel, low, preferred_element_type=jnp.float32)


def product(a, b):
    return jnp.dot(a, b, preferred_element_type=jnp.float32)


def per_device(probes, own_blocks, cross_blocks, level_perm):
    col_bits = lax.axis_size("col").bit_length() - 1
    row_bits = lax.axis_size("row").bit_length() - 1
    z_bit, hi_bit, lo_bit = col_bits - 1, row_bits - 1, 0
    br = own_blocks.shape[1]
    weights = []
    for level in range(3):
        both = jnp.concatenate([own_blocks[level], cross_blocks[level]], axis=0)
        both = permuted_columns(both, level_perm[level])
        weights.append((both[:br], both[br:]))
    (own0, cross0), (own1, cross1), (own2, cross2) = weights
    theirs = from_partner(jnp.stack([cross2, cross1, own2]), "col", lo_bit)
    k_self = split(product(own1, own2))
    k_diag = split(product(theirs[1], cross2))
    k_to_p = split(product(own1, theirs[0]))
    k_diag_p = split(product(theirs[1], theirs[2]))
    rows = probes.shape[0] // CHUNKS
    outs = []
    for chunk in range(CHUNKS):
        panel = probes[chunk * rows:(chunk + 1) * rows]
        other = from_partner(panel, "col", z_bit)
        (k_self, k_diag, k_to_p, k_diag_p), other = lax.optimization_barrier(((k_self, k_diag, k_to_p, k_diag_p), other))
        total = jnp.dot(panel, own0, preferred_element_type=jnp.float32)
        total = total + jnp.dot(other, cross0, preferred_element_type=jnp.float32)
        panel = total.astype(jnp.bfloat16)
        diag = from_diagonal(panel, hi_bit, lo_bit)
        share = (times(panel, k_to_p) + times(diag, k_diag_p)).astype(jnp.bfloat16)
        received = from_partner(share, "col", lo_bit)
        total = times(panel, k_self) + times(diag, k_diag)
        outs.append((total + received.astype(jnp.float32)).astype(jnp.bfloat16))
    return jnp.concatenate(outs, axis=0)


def solution(mesh):
    placed = (
        P(None, ("row", "col")),
        P(None, ("row", "col"), None),
        P(None, ("row", "col"), None),
        P(None, ("row", "col")),
    )
    return jax.shard_map(
        per_device, mesh=mesh, in_specs=placed, out_specs=P(None, ("row", "col")), check_vma=False
    )
```

```python
import jax
import jax.numpy as jnp
from jax import lax
from jax.sharding import PartitionSpec as P

CHUNKS = 2


def from_partner(value, axis, distance):
    mask = 2**distance
    pairs = [(source, source ^ mask) for source in range(lax.axis_size(axis))]
    return lax.ppermute(value, axis, pairs)


def from_diagonal(value, row_bit, col_bit):
    rows, cols = lax.axis_size("row"), lax.axis_size("col")
    pairs = [
        (r * cols + c, (r ^ 2**row_bit) * cols + (c ^ 2**col_bit)) for r in range(rows) for c in range(cols)
    ]
    return lax.ppermute(value, ("row", "col"), pairs)


def combine(panel, partner, own, cross):
    total = jnp.dot(panel, own, preferred_element_type=jnp.float32)
    total = total + jnp.dot(partner, cross, preferred_element_type=jnp.float32)
    return total.astype(jnp.bfloat16)


def permuted_columns(weights, order):
    n = weights.shape[-1]
    onehot = (lax.broadcasted_iota(jnp.int32, (n, n), 0) == order[None, :]).astype(weights.dtype)
    return jnp.dot(weights, onehot, preferred_element_type=jnp.float32).astype(weights.dtype)


def per_device(probes, own_blocks, cross_blocks, level_perm):
    col_bits = lax.axis_size("col").bit_length() - 1
    row_bits = lax.axis_size("row").bit_length() - 1
    plan = [("col", col_bits - 1), ("row", row_bits - 1), ("col", 0)]
    br = own_blocks.shape[1]
    weights = []
    for level in range(3):
        both = jnp.concatenate([own_blocks[level], cross_blocks[level]], axis=0)
        both = permuted_columns(both, level_perm[level])
        weights.append((both[:br], both[br:]))
    (own0, cross0), (own1, cross1), (own2, cross2) = weights
    z_bit, hi_bit, lo_bit = plan[0][1], plan[1][1], plan[2][1]
    theirs = from_partner(jnp.stack([own1, cross1]), "col", lo_bit)
    rows = probes.shape[0] // CHUNKS
    outs = []
    for chunk in range(CHUNKS):
        panel = probes[chunk * rows:(chunk + 1) * rows]
        panel = combine(panel, from_partner(panel, "col", z_bit), own0, cross0)
        far = from_partner(panel, "row", hi_bit)
        near = from_partner(panel, "col", lo_bit)
        diag = from_diagonal(panel, hi_bit, lo_bit)
        mine = combine(panel, far, own1, cross1)
        partners = combine(near, diag, theirs[0], theirs[1])
        outs.append(combine(mine, partners, own2, cross2))
    return jnp.concatenate(outs, axis=0)


def solution(mesh):
    placed = (
        P(None, ("row", "col")),
        P(None, ("row", "col"), None),
        P(None, ("row", "col"), None),
        P(None, ("row", "col")),
    )
    return jax.shard_map(
        per_device, mesh=mesh, in_specs=placed, out_specs=P(None, ("row", "col")), check_vma=False
    )
```

```python
import jax
import jax.numpy as jnp
from jax import lax
from jax.sharding import PartitionSpec as P

CHUNKS = 2


def from_partner(value, axis, distance):
    mask = 2**distance
    pairs = [(source, source ^ mask) for source in range(lax.axis_size(axis))]
    return lax.ppermute(value, axis, pairs)


def permuted_columns(weights, order):
    n = weights.shape[-1]
    onehot = (lax.broadcasted_iota(jnp.int32, (n, n), 0) == order[None, :]).astype(weights.dtype)
    return jnp.dot(weights, onehot, preferred_element_type=jnp.float32).astype(weights.dtype)


def per_device(probes, own_blocks, cross_blocks, level_perm):
    col_bits = lax.axis_size("col").bit_length() - 1
    row_bits = lax.axis_size("row").bit_length() - 1
    plan = [("col", col_bits - 1), ("row", row_bits - 1), ("col", 0)]
    br = own_blocks.shape[1]
    weights = []
    for level in range(3):
        both = jnp.concatenate([own_blocks[level], cross_blocks[level]], axis=0)
        both = permuted_columns(both, level_perm[level])
        weights.append((both[:br], both[br:]))
    rows = probes.shape[0] // CHUNKS
    outs = []
    source = probes
    for chunk in range(CHUNKS):
        panel = source[chunk * rows:(chunk + 1) * rows]
        panel, source = lax.optimization_barrier((panel, source))
        for level, (axis, bit) in enumerate(plan):
            own, cross = weights[level]
            other = from_partner(panel, axis, bit)
            total = jnp.dot(panel, own, preferred_element_type=jnp.float32)
            total = total + jnp.dot(other, cross, preferred_element_type=jnp.float32)
            panel = total.astype(jnp.bfloat16)
        outs.append(panel)
    return jnp.concatenate(outs, axis=0)


def solution(mesh):
    placed = (
        P(None, ("row", "col")),
        P(None, ("row", "col"), None),
        P(None, ("row", "col"), None),
        P(None, ("row", "col")),
    )
    return jax.shard_map(
        per_device, mesh=mesh, in_specs=placed, out_specs=P(None, ("row", "col")), check_vma=False
    )
```

```python
import jax
import jax.numpy as jnp
from jax import lax
from jax.sharding import PartitionSpec as P

CHUNKS = 2


def from_partner(value, axis, distance):
    mask = 2**distance
    pairs = [(source, source ^ mask) for source in range(lax.axis_size(axis))]
    return lax.ppermute(value, axis, pairs)


def permuted_columns(weights, order):
    n = weights.shape[-1]
    onehot = (lax.broadcasted_iota(jnp.int32, (n, n), 0) == order[None, :]).astype(weights.dtype)
    return jnp.dot(weights, onehot, preferred_element_type=jnp.float32).astype(weights.dtype)


def per_device(probes, own_blocks, cross_blocks, level_perm):
    col_bits = lax.axis_size("col").bit_length() - 1
    row_bits = lax.axis_size("row").bit_length() - 1
    plan = [("col", col_bits - 1), ("row", row_bits - 1), ("col", 0)]
    br = own_blocks.shape[1]
    weights = []
    for level in range(3):
        both = jnp.concatenate([own_blocks[level], cross_blocks[level]], axis=0)
        both = permuted_columns(both, level_perm[level])
        weights.append((both[:br], both[br:]))
    rows = probes.shape[0] // CHUNKS
    outs = []
    source = probes
    for chunk in range(CHUNKS):
        panel = source[chunk * rows:(chunk + 1) * rows]
        panel, source = lax.optimization_barrier((panel, source))
        for level, (axis, bit) in enumerate(plan):
            own, cross = weights[level]
            other = from_partner(panel, axis, bit)
            total = jnp.dot(panel, own, preferred_element_type=jnp.float32)
            total = total + jnp.dot(other, cross, preferred_element_type=jnp.float32)
            panel = total.astype(jnp.bfloat16)
        outs.append(panel)
    result = jnp.zeros(probes.shape, probes.dtype)
    for chunk, panel in enumerate(outs):
        result = lax.dynamic_update_slice(result, panel, (chunk * rows, 0))
        if chunk + 1 < CHUNKS:
            result = lax.optimization_barrier(result)
    return result


def solution(mesh):
    placed = (
        P(None, ("row", "col")),
        P(None, ("row", "col"), None),
        P(None, ("row", "col"), None),
        P(None, ("row", "col")),
    )
    return jax.shard_map(
        per_device, mesh=mesh, in_specs=placed, out_specs=P(None, ("row", "col")), check_vma=False
    )
```

```python
import jax
import jax.numpy as jnp
from jax import lax
from jax.sharding import PartitionSpec as P

CHUNKS = 2


def from_partner(value, axis, distance):
    mask = 2**distance
    pairs = [(source, source ^ mask) for source in range(lax.axis_size(axis))]
    return lax.ppermute(value, axis, pairs)


def permuted_columns(weights, order):
    n = weights.shape[-1]
    onehot = (lax.broadcasted_iota(jnp.int32, (n, n), 0) == order[None, :]).astype(weights.dtype)
    return jnp.dot(weights, onehot, preferred_element_type=jnp.float32).astype(weights.dtype)


def per_device(probes, own_blocks, cross_blocks, level_perm):
    col_bits = lax.axis_size("col").bit_length() - 1
    row_bits = lax.axis_size("row").bit_length() - 1
    plan = [("col", col_bits - 1), ("row", row_bits - 1), ("col", 0)]
    br = own_blocks.shape[1]
    weights = []
    for level in range(3):
        both = jnp.concatenate([own_blocks[level], cross_blocks[level]], axis=0)
        both = permuted_columns(both, level_perm[level])
        weights.append((both[:br], both[br:]))
    rows = probes.shape[0] // CHUNKS
    outs = []
    source = probes
    for chunk in range(CHUNKS):
        panel = source[chunk * rows:(chunk + 1) * rows]
        panel, source = lax.optimization_barrier((panel, source))
        for level, (axis, bit) in enumerate(plan):
            own, cross = weights[level]
            total = jnp.dot(panel, own, preferred_element_type=jnp.float32)
            if level > 0 and chunk + 1 < CHUNKS:
                panel, total = lax.optimization_barrier((panel, total))
            other = from_partner(panel, axis, bit)
            total = total + jnp.dot(other, cross, preferred_element_type=jnp.float32)
            panel = total.astype(jnp.bfloat16)
        outs.append(panel)
    return jnp.concatenate(outs, axis=0)


def solution(mesh):
    placed = (
        P(None, ("row", "col")),
        P(None, ("row", "col"), None),
        P(None, ("row", "col"), None),
        P(None, ("row", "col")),
    )
    return jax.shard_map(
        per_device, mesh=mesh, in_specs=placed, out_specs=P(None, ("row", "col")), check_vma=False
    )
```

```python
import jax
import jax.numpy as jnp
from jax import lax
from jax.sharding import PartitionSpec as P

SPLIT = (3, 5)


def from_partner(value, axis, distance):
    mask = 2**distance
    pairs = [(source, source ^ mask) for source in range(lax.axis_size(axis))]
    return lax.ppermute(value, axis, pairs)


def permuted_columns(weights, order):
    n = weights.shape[-1]
    onehot = (lax.broadcasted_iota(jnp.int32, (n, n), 0) == order[None, :]).astype(weights.dtype)
    return jnp.dot(weights, onehot, preferred_element_type=jnp.float32).astype(weights.dtype)


def per_device(probes, own_blocks, cross_blocks, level_perm):
    col_bits = lax.axis_size("col").bit_length() - 1
    row_bits = lax.axis_size("row").bit_length() - 1
    plan = [("col", col_bits - 1), ("row", row_bits - 1), ("col", 0)]
    br = own_blocks.shape[1]
    weights = []
    for level in range(3):
        both = jnp.concatenate([own_blocks[level], cross_blocks[level]], axis=0)
        both = permuted_columns(both, level_perm[level])
        weights.append((both[:br], both[br:]))
    unit = probes.shape[0] // sum(SPLIT)
    bounds = [unit * sum(SPLIT[:k]) for k in range(len(SPLIT) + 1)]
    panels = []
    source = probes
    for chunk in range(len(SPLIT)):
        panel, source = lax.optimization_barrier((source[bounds[chunk]:bounds[chunk + 1]], source))
        panels.append(panel)
    arrived = [from_partner(panel, *plan[0]) for panel in panels]
    outs = []
    for chunk in range(len(SPLIT)):
        panel = panels[chunk]
        for level, (axis, bit) in enumerate(plan):
            own, cross = weights[level]
            other = arrived[chunk] if level == 0 else from_partner(panel, axis, bit)
            if level == 2 and chunk + 1 < len(SPLIT):
                panel, arrived[chunk + 1] = lax.optimization_barrier((panel, arrived[chunk + 1]))
            total = jnp.dot(panel, own, preferred_element_type=jnp.float32)
            total = total + jnp.dot(other, cross, preferred_element_type=jnp.float32)
            panel = total.astype(jnp.bfloat16)
        outs.append(panel)
    return jnp.concatenate(outs, axis=0)


def solution(mesh):
    placed = (
        P(None, ("row", "col")),
        P(None, ("row", "col"), None),
        P(None, ("row", "col"), None),
        P(None, ("row", "col")),
    )
    return jax.shard_map(
        per_device, mesh=mesh, in_specs=placed, out_specs=P(None, ("row", "col")), check_vma=False
    )
```
